512 devices in a mesh: req: 64 (over y, x, core), tp: 8 (over z).
Axes of the slice: x: 4, y: 8, z: 8, core: 2. Of those that a mesh axis runs over, the one named last changes fastest.
Arguments:
- tokens: bfloat16 [8192, 8192], P('req', 'tp'), may hold values from -6 to 6
- kv_weight: bfloat16 [8192, 1024], P('tp'), may hold values from -0.0625 to 0.0625
- queries: bfloat16 [8192, 4096], P('req', 'tp'), may hold values from -96 to 96, as said below
- lengths: int32 [32], replicated, may hold values from 1 to 384, 8192 in all
- page_owner: int32 [4096, 1], P('req'), may hold values from 0 to 63; in each aligned block of 64 rows (0 to 63, 64 to 127, ...) at most 2 rows name the same one
Outputs:
- attended: bfloat16 [8192, 4096], P('req', 'tp')
- cache: bfloat16 [16384, 1024], P('req', 'tp')
The draws below stay inside these ranges and needn't reach their ends.
Inputs may be any that keep to these rules, and one draw needn't show every extreme that they name: `queries`: real values; entries of a row share a scale. The 32 lengths sum to 8192; the largest is exactly 384. `page_owner`: among the 64 pages of one device no owner is named more than 2 times, a bound that some block reaches.
All inputs are finite; a program needn't handle non-finite values.
Results may differ from the reference program's by a relative error of at most 0.012.
Values may be sent and summed in bfloat16 or wider, within the bound.
No kernel may reach another device: no remote copies, remote signals or barrier semaphores. Data moves between devices by JAX's collectives and lax.ppermute only.
A program may use at most 64 MiB of HBM per device.

```python
import math
import jax
import jax.numpy as jnp
import numpy as np
from jax import lax

D = 8192
HD = 128
HQ = 32
KVH = 4
BACK = 3
PAGES_DEV = 64
TOK_DEV = 128
TOKENS = 8192
SEGS = 32
MOST = 384
PAGE = 2
PAGES = 4096
CAP = 2
CACHE_DEV = 256
N_REQ = 64


def draw_queries(key, part):
    base = jnp.clip(jax.random.normal(key, (TOKENS, HQ * HD), jnp.float32), -6.0, 6.0)
    return base.astype(jnp.bfloat16)


def steps_of(stream_key, shape, pieces, low, high):
    factor_of, own = 1.0, jax.random.fold_in(stream_key, 6)
    for axis_at, shards_of in pieces:
        steps = jnp.exp(jax.random.uniform(jax.random.fold_in(own, axis_at), (shards_of,), jnp.float32, low / len(pieces), high / len(pieces)))
        factor_of = factor_of * jnp.repeat(steps, shape[axis_at] // shards_of).reshape([-1 if axis == axis_at else 1 for axis in range(len(shape))])
    return factor_of


def split_up(number_of, total, most, slope):
    loads = [(1 << 20) // math.isqrt(standing ** slope) + 1 for standing in range(2, number_of + 1)]
    spare, given = total - most - (number_of - 1), [1] * (number_of - 1)
    while spare > 0:
        candidates = [i for i in range(number_of - 1) if given[i] < most]
        pool, budget = sum([loads[i] for i in candidates]), spare
        for i in candidates:
            addition = min(most - given[i], max(1, budget * loads[i] // pool), spare)
            given[i] = given[i] + addition
            spare = spare - addition
    return np.array([most] + given)


def ragged_sizes(key, count, total, limit, lean):
    if count == 2:
        one = jax.random.randint(key, (), max(1, total - limit), min(limit, total - 1) + 1)
        return jnp.stack([one, total - one])
    sizes = jnp.asarray(split_up(count, total, limit, lean), jnp.int32)
    couples = (count - 1) // 2
    source_of, sink = sizes[1:1 + 2 * couples:2], sizes[2:2 + 2 * couples:2]
    margin = jnp.minimum(source_of - 1, limit - sink)
    shifted = jax.random.randint(jax.random.fold_in(key, 1), (couples,), 0, 1 << 20) % (margin + 1)
    sizes = sizes.at[1:1 + 2 * couples:2].set(source_of - shifted).at[2:2 + 2 * couples:2].set(sink + shifted)
    return sizes[jax.random.permutation(jax.random.fold_in(key, 2), count)]


def routed_block(key, own, number, rows, count, top, bound, skew):
    ranking = jax.random.permutation(key, count)
    crowded, common = portions_of(count, rows * top, bound, skew, True), portions_of(count, rows * top, bound, skew, False)
    places = jnp.arange(count)

    def named(sizes, rotation):
        used = int((sizes > 0).sum())
        fixed = max(1, used // 4)
        passed = fixed + (places - fixed + rotation * (used - fixed)) % max(1, count - fixed)
        return jnp.zeros((count,), jnp.int32).at[ranking[jnp.where(places < fixed, places, passed)]].set(jnp.asarray(sizes, jnp.int32))

    sizes = jnp.where(number % 4 == 0, named(crowded, number // 4), named(common, number - number // 4 - 1))
    mixed = jax.random.permutation(jax.random.fold_in(own, 3), count)
    source_of, sink = mixed[0:count // 2 * 2:2], mixed[1:count // 2 * 2:2]
    room = jnp.minimum(sizes[source_of] - 1, bound - sizes[sink]) // 2
    room = jnp.where((source_of == ranking[0]) | (sink == ranking[0]) | (sizes[sink] == 0), 0, jnp.maximum(room, 0))
    passed = jax.random.randint(jax.random.fold_in(own, 4), (count // 2,), 0, 1 << 20) % (room + 1)
    sizes = sizes.at[source_of].add(-passed).at[sink].add(passed)
    members = jnp.searchsorted(jnp.cumsum(sizes), jnp.arange(rows * top), side="right").astype(jnp.int32)
    listing = members.reshape(top, rows).T
    listing = listing[jax.random.permutation(jax.random.fold_in(own, 1), rows)]
    rotation = jax.random.randint(jax.random.fold_in(own, 2), (rows, 1), 0, top)
    return jnp.take_along_axis(listing, (jnp.arange(top)[None, :] + rotation) % top, axis=1)


def portions_of(number_of, total, limit, slope, full):
    portions = [(1 << 20) // math.isqrt(grade ** slope) + 1 for grade in range(1, number_of + 1)]
    largest = limit if full else min(limit, max(-(-total // number_of), total * portions[0] // sum(portions)))
    least = 1 if total - largest >= number_of - 1 else 0
    holding, spare = [largest] + [least] * (number_of - 1), total - largest - least * (number_of - 1)
    while spare > 0:
        candidates = [i for i in range(1, number_of) if holding[i] < largest] or [i for i in range(1, number_of) if holding[i] < limit]
        pool, remaining = sum([portions[i] for i in candidates]), spare
        for i in candidates:
            addition = min(limit - holding[i], max(1, remaining * portions[i] // pool), spare)
            holding[i] = holding[i] + addition
            spare = spare - addition
    return np.array(holding)


def scatter_about(key, shape, scale, most, pieces=(), held_as=jnp.bfloat16):
    gain = steps_of(key, shape, pieces, -0.22, 0.18) if pieces else 1.0
    values = jax.random.normal(key, shape, jnp.float32) * scale * gain
    return jnp.minimum(jnp.maximum(values, -most), most).astype(held_as)


def setup_inputs(seed: int = 0) -> dict:
    key_list = jax.random.split(jax.random.key(seed), 6)
    tokens = scatter_about(key_list[0], (TOKENS, D), 1.0, 6.0, ((0, 64), (1, 8)))
    kv_weight = scatter_about(key_list[1], (D, 2 * KVH * HD), D ** -0.5, 0.0625, ((0, 8),))
    queries = draw_queries(jax.random.fold_in(key_list[5], 71), 0)
    lengths = ragged_sizes(key_list[3], SEGS, TOKENS, MOST, 2).astype(jnp.int32)
    page_owner_keys = jax.random.split(jax.random.fold_in(key_list[4], 1), PAGES // PAGES_DEV)
    page_owner_turns = jax.random.permutation(jax.random.fold_in(key_list[4], 3), PAGES // PAGES_DEV)
    page_owner = jax.vmap(lambda own, number: routed_block(jax.random.fold_in(key_list[4], 2), own, number, PAGES_DEV, N_REQ, 1, CAP, 2))(page_owner_keys, page_owner_turns).reshape((PAGES, 1))
    return {"tokens": tokens, "kv_weight": kv_weight, "queries": queries, "lengths": lengths, "page_owner": page_owner}


rope_base = 500000.0

def rotate(values, positions):
    middle = HD // 2
    frequency = rope_base ** (-(2.0 * jnp.arange(middle, dtype=jnp.float32)) / HD)
    angles = positions.astype(jnp.float32)[:, None] * frequency[None, :]
    cosine = jnp.cos(angles)[:, None, :]
    sine = jnp.sin(angles)[:, None, :]
    front = values[..., :middle]
    behind = values[..., middle:]
    return jnp.concatenate([front * cosine - behind * sine, behind * cosine + front * sine], axis=-1)

def segment_info(lengths, indices):
    ends = jnp.cumsum(lengths)
    before = ends[None, :] <= indices[:, None]
    segment = lax.optimization_barrier(jnp.sum(before.astype(jnp.int32), axis=1))
    start = lax.optimization_barrier(jnp.sum(jnp.where(before, lengths[None, :], 0), axis=1))
    return (segment, indices - start)

def reference(tokens, kv_weight, queries, lengths, page_owner):
    columns = 2 * KVH * HD
    summed = jnp.dot(tokens, kv_weight, preferred_element_type=jnp.float32)
    everywhere = jnp.arange(TOKENS, dtype=jnp.int32)
    segment, positions = segment_info(lengths, everywhere)
    heads = summed.reshape(TOKENS, KVH, 2, HD)
    keys = rotate(heads[:, :, 0, :], positions).astype(jnp.bfloat16)
    values = heads[:, :, 1, :].astype(jnp.bfloat16)
    cache_rows = jnp.stack([keys, values], axis=2).reshape(TOKENS, columns)
    rotated = rotate(queries.astype(jnp.float32).reshape(TOKENS, HQ, HD), positions).astype(jnp.bfloat16)
    group = HQ // KVH
    reach = BACK * TOK_DEV
    padded_keys = jnp.concatenate([jnp.zeros((reach, KVH, HD), jnp.bfloat16), keys], axis=0)
    padded_values = jnp.concatenate([jnp.zeros((reach, KVH, HD), jnp.bfloat16), values], axis=0)

    def attend(block):
        begin = block * TOK_DEV
        query_block = lax.dynamic_slice_in_dim(rotated, begin, TOK_DEV, 0).astype(jnp.float32)
        key_block = jnp.repeat(lax.dynamic_slice_in_dim(padded_keys, begin, reach + TOK_DEV, 0), group, axis=1).astype(jnp.float32)
        value_block = jnp.repeat(lax.dynamic_slice_in_dim(padded_values, begin, reach + TOK_DEV, 0), group, axis=1).astype(jnp.float32)
        scores = jnp.einsum('qhd,khd->hqk', query_block, key_block) / math.sqrt(HD)
        query_index = begin + jnp.arange(TOK_DEV, dtype=jnp.int32)
        key_index = begin - reach + jnp.arange(reach + TOK_DEV, dtype=jnp.int32)
        query_segment, unused = segment_info(lengths, query_index)
        key_segment, unused_too = segment_info(lengths, key_index)
        allowed = (key_index[None, :] >= 0) & (key_index[None, :] <= query_index[:, None]) & (key_segment[None, :] == query_segment[:, None])
        scores = jnp.where(allowed[None], scores, -1e+30)
        largest = lax.optimization_barrier(jnp.max(scores, axis=2, keepdims=True))
        weights = jnp.exp(scores - largest)
        total = lax.optimization_barrier(jnp.sum(weights, axis=2, keepdims=True))
        probabilities = lax.optimization_barrier(weights.astype(jnp.bfloat16)).astype(jnp.float32)
        mixed = jnp.einsum('hqk,khd->hqd', probabilities, value_block)
        result = (mixed / total).astype(jnp.bfloat16)
        return jnp.transpose(result, (1, 0, 2)).reshape(TOK_DEV, HQ * HD)
    attended = lax.map(attend, jnp.arange(N_REQ, dtype=jnp.int32)).reshape(TOKENS, HQ * HD)
    owners = page_owner.reshape(N_REQ, PAGES_DEV)
    order = jnp.arange(PAGES_DEV, dtype=jnp.int32)
    earlier = (owners[:, :, None] == owners[:, None, :]) & (order[None, :] < order[:, None])[None]
    rank = lax.optimization_barrier(jnp.sum(earlier.astype(jnp.int32), axis=2))
    source = jnp.broadcast_to(jnp.arange(N_REQ, dtype=jnp.int32)[:, None], owners.shape)
    pages = cache_rows.reshape(N_REQ, PAGES_DEV, PAGE * columns)
    cache = jnp.zeros((N_REQ, N_REQ, CAP, PAGE * columns), jnp.bfloat16).at[owners, source, rank].set(pages)
    cache = cache.reshape(N_REQ * CACHE_DEV, columns)
    return (attended, cache)
```

```python
import math

import jax
import jax.numpy as jnp
from jax import lax
from jax.sharding import PartitionSpec as P

HD = 128
HQ = 32
KVH = 4
BACK = 3


rope_base = 500000.0


def shifted(value, axis, steps):
    count = lax.axis_size(axis)
    first, last = (max(0, -steps), min(count, count - steps))
    return lax.ppermute(value, axis, [(source, source + steps) for source in range(first, last)])


def rotate(values, positions):
    middle = HD // 2
    frequency = rope_base ** (-(2.0 * jnp.arange(middle, dtype=jnp.float32)) / HD)
    angles = positions.astype(jnp.float32)[:, None] * frequency[None, :]
    cosine = jnp.cos(angles)[:, None, :]
    sine = jnp.sin(angles)[:, None, :]
    front = values[..., :middle]
    behind = values[..., middle:]
    return jnp.concatenate(
        [front * cosine - behind * sine, behind * cosine + front * sine], axis=-1
    )


def segment_info(lengths, indices):
    ends = jnp.cumsum(lengths)
    before = ends[None, :] <= indices[:, None]
    segment = jnp.sum(before.astype(jnp.int32), axis=1)
    start = jnp.sum(jnp.where(before, lengths[None, :], 0), axis=1)
    return (segment, indices - start)


def local(tokens, kv_weight, queries, lengths, page_owner):
    rows = tokens.shape[0]
    tp_size = lax.axis_size("tp")
    tp_index = lax.axis_index("tp")
    req_index = lax.axis_index("req")
    local_index = req_index * rows + jnp.arange(rows, dtype=jnp.int32)
    segment, positions = segment_info(lengths, local_index)
    local_heads = queries.shape[1] // HD
    partial_value = jnp.dot(tokens, kv_weight, preferred_element_type=jnp.float32)
    own = lax.psum_scatter(partial_value, "tp", scatter_dimension=1, tiled=True)
    is_key = tp_index % 2 == 0
    turned = rotate(own.reshape(rows, 1, HD), positions).reshape(rows, HD)
    mine = jnp.where(is_key, turned, own).astype(jnp.bfloat16)
    other = lax.ppermute(mine, "tp", [(i, i ^ 1) for i in range(tp_size)])
    key_now = jnp.where(is_key, mine, other)
    value_now = jnp.where(is_key, other, mine)
    near = jnp.concatenate([key_now, value_now], axis=1)
    rotated = rotate(queries.astype(jnp.float32).reshape(rows, local_heads, HD), positions).astype(
        jnp.bfloat16
    )
    blocks = []
    for distance in range(BACK, 0, -1):
        blocks.append(shifted(near, "req", distance))
    blocks.append(near)
    window = jnp.concatenate(blocks, axis=0)
    key_total = (BACK + 1) * rows
    key_index = (req_index - BACK) * rows + jnp.arange(key_total, dtype=jnp.int32)
    key_segment, unused = segment_info(lengths, key_index)
    allowed = (
        (key_index[None, :] >= 0)
        & (key_index[None, :] <= local_index[:, None])
        & (key_segment[None, :] == segment[:, None])
    )
    key_head = window[:, :HD]
    value_head = window[:, HD:]
    query_heads = jnp.transpose(rotated, (1, 0, 2))
    scores = lax.dot_general(
        query_heads, key_head, (((2,), (1,)), ((), ())), preferred_element_type=jnp.float32
    ) / math.sqrt(HD)
    scores = jnp.where(allowed[None], scores, -1e30)
    largest = jnp.max(scores, axis=2, keepdims=True)
    weights = jnp.exp(scores - largest)
    total = jnp.sum(weights, axis=2, keepdims=True)
    mixed = lax.dot_general(
        weights.astype(jnp.bfloat16), value_head, (((2,), (0,)), ((), ())),
        preferred_element_type=jnp.float32,
    )
    outputs = (mixed / total).astype(jnp.bfloat16)
    attended = jnp.transpose(outputs, (1, 0, 2)).reshape(rows, local_heads * HD)
    share = mine.shape[1]
    pages_here = page_owner.shape[0]
    owners = page_owner[:, 0]
    page_rows = rows // pages_here
    capacity = 2 * pages_here // lax.axis_size("req")
    order = jnp.arange(pages_here, dtype=jnp.int32)
    earlier = (owners[:, None] == owners[None, :]) & (order[None, :] < order[:, None])
    rank = jnp.sum(earlier.astype(jnp.int32), axis=1)
    target = owners * capacity + rank
    slots = lax.axis_size("req") * capacity
    placing = (jnp.arange(slots, dtype=jnp.int32)[:, None] == target[None, :]).astype(jnp.bfloat16)
    paged = mine.reshape(pages_here, page_rows * share)
    outgoing = jnp.dot(placing, paged, preferred_element_type=jnp.float32).astype(jnp.bfloat16)
    incoming = lax.all_to_all(outgoing, "req", split_axis=0, concat_axis=0, tiled=True)
    cache = incoming.reshape(slots * page_rows, share)
    return (attended, cache)


def solution(mesh):
    in_specs = (P("req", "tp"), P("tp", None), P("req", "tp"), P(), P("req", None))
    out_specs = (P("req", "tp"), P("req", "tp"))
    return jax.shard_map(local, mesh=mesh, in_specs=in_specs, out_specs=out_specs, check_vma=False)
```

```python
import math

import jax
import jax.numpy as jnp
from jax import lax
from jax.sharding import PartitionSpec as P

HD = 128
HQ = 32
KVH = 4
BACK = 3


rope_base = 500000.0


def shifted(value, axis, steps):
    count = lax.axis_size(axis)
    first, last = (max(0, -steps), min(count, count - steps))
    return lax.ppermute(value, axis, [(source, source + steps) for source in range(first, last)])


def rotate(values, positions):
    middle = HD // 2
    frequency = rope_base ** (-(2.0 * jnp.arange(middle, dtype=jnp.float32)) / HD)
    angles = positions.astype(jnp.float32)[:, None] * frequency[None, :]
    cosine = jnp.cos(angles)[:, None, :]
    sine = jnp.sin(angles)[:, None, :]
    front = values[..., :middle]
    behind = values[..., middle:]
    return jnp.concatenate(
        [front * cosine - behind * sine, behind * cosine + front * sine], axis=-1
    )


def segment_info(lengths, indices):
    ends = jnp.cumsum(lengths)
    before = ends[None, :] <= indices[:, None]
    segment = jnp.sum(before.astype(jnp.int32), axis=1)
    start = jnp.sum(jnp.where(before, lengths[None, :], 0), axis=1)
    return (segment, indices - start)


def local(tokens, kv_weight, queries, lengths, page_owner):
    rows = tokens.shape[0]
    tp_size = lax.axis_size("tp")
    tp_index = lax.axis_index("tp")
    req_index = lax.axis_index("req")
    local_index = req_index * rows + jnp.arange(rows, dtype=jnp.int32)
    segment, positions = segment_info(lengths, local_index)
    local_heads = queries.shape[1] // HD
    partial_value = jnp.dot(tokens, kv_weight, preferred_element_type=jnp.float32)
    heads_here = partial_value.shape[1] // (2 * HD)
    per_head = tp_size // heads_here
    pieces = partial_value.astype(jnp.bfloat16).reshape(rows, heads_here, 2 * HD)
    pieces = jnp.repeat(jnp.transpose(pieces, (1, 0, 2)), per_head, axis=0)
    arrived = lax.all_to_all(pieces, "tp", 0, 0, tiled=True)
    head_sum = jnp.sum(arrived.astype(jnp.float32), axis=0)
    key_now = rotate(head_sum[:, :HD].reshape(rows, 1, HD), positions).reshape(rows, HD)
    near = jnp.concatenate([key_now, head_sum[:, HD:]], axis=1).astype(jnp.bfloat16)
    mine = lax.dynamic_slice_in_dim(near, (tp_index % per_head) * HD, HD, 1)
    rotated = rotate(queries.astype(jnp.float32).reshape(rows, local_heads, HD), positions).astype(
        jnp.bfloat16
    )
    blocks = []
    for distance in range(BACK, 0, -1):
        blocks.append(shifted(near, "req", distance))
    blocks.append(near)
    window = jnp.concatenate(blocks, axis=0)
    key_total = (BACK + 1) * rows
    key_index = (req_index - BACK) * rows + jnp.arange(key_total, dtype=jnp.int32)
    key_segment, unused = segment_info(lengths, key_index)
    allowed = (
        (key_index[None, :] >= 0)
        & (key_index[None, :] <= local_index[:, None])
        & (key_segment[None, :] == segment[:, None])
    )
    key_head = window[:, :HD]
    value_head = window[:, HD:]
    query_heads = jnp.transpose(rotated, (1, 0, 2))
    scores = lax.dot_general(
        query_heads, key_head, (((2,), (1,)), ((), ())), preferred_element_type=jnp.float32
    ) / math.sqrt(HD)
    scores = jnp.where(allowed[None], scores, -1e30)
    largest = jnp.max(scores, axis=2, keepdims=True)
    weights = jnp.exp(scores - largest)
    total = jnp.sum(weights, axis=2, keepdims=True)
    mixed = lax.dot_general(
        weights.astype(jnp.bfloat16), value_head, (((2,), (0,)), ((), ())),
        preferred_element_type=jnp.float32,
    )
    outputs = (mixed / total).astype(jnp.bfloat16)
    attended = jnp.transpose(outputs, (1, 0, 2)).reshape(rows, local_heads * HD)
    share = mine.shape[1]
    pages_here = page_owner.shape[0]
    owners = page_owner[:, 0]
    page_rows = rows // pages_here
    capacity = 2 * pages_here // lax.axis_size("req")
    order = jnp.arange(pages_here, dtype=jnp.int32)
    earlier = (owners[:, None] == owners[None, :]) & (order[None, :] < order[:, None])
    rank = jnp.sum(earlier.astype(jnp.int32), axis=1)
    target = owners * capacity + rank
    slots = lax.axis_size("req") * capacity
    placing = (jnp.arange(slots, dtype=jnp.int32)[:, None] == target[None, :]).astype(jnp.bfloat16)
    paged = mine.reshape(pages_here, page_rows * share)
    outgoing = jnp.dot(placing, paged, preferred_element_type=jnp.float32).astype(jnp.bfloat16)
    incoming = lax.all_to_all(outgoing, "req", split_axis=0, concat_axis=0, tiled=True)
    cache = incoming.reshape(slots * page_rows, share)
    return (attended, cache)


def solution(mesh):
    in_specs = (P("req", "tp"), P("tp", None), P("req", "tp"), P(), P("req", None))
    out_specs = (P("req", "tp"), P("req", "tp"))
    return jax.shard_map(local, mesh=mesh, in_specs=in_specs, out_specs=out_specs, check_vma=False)
```

```python
import math

import jax
import jax.numpy as jnp
from jax import lax
from jax.sharding import PartitionSpec as P


HD = 128
BACK = 3


rope_base = 500000.0


def shifted(value, axis, steps):
    count = lax.axis_size(axis)
    first, last = (max(0, -steps), min(count, count - steps))
    return lax.ppermute(value, axis, [(source, source + steps) for source in range(first, last)])


def rotate(values, positions):
    middle = HD // 2
    frequency = rope_base ** (-(2.0 * jnp.arange(middle, dtype=jnp.float32)) / HD)
    angles = positions.astype(jnp.float32)[:, None] * frequency[None, :]
    cosine = jnp.cos(angles)[:, None, :]
    sine = jnp.sin(angles)[:, None, :]
    front = values[..., :middle]
    behind = values[..., middle:]
    return jnp.concatenate(
        [front * cosine - behind * sine, behind * cosine + front * sine], axis=-1
    )


def segment_info(lengths, indices):
    ends = jnp.cumsum(lengths)
    before = ends[None, :] <= indices[:, None]
    segment = jnp.sum(before.astype(jnp.int32), axis=1)
    start = jnp.sum(jnp.where(before, lengths[None, :], 0), axis=1)
    return (segment, indices - start)


def layer(tokens, kv_weight, queries, lengths, page_owner):
    rows = tokens.shape[0]
    tp_size = lax.axis_size("tp")
    tp_index = lax.axis_index("tp")
    req_index = lax.axis_index("req")
    local_index = req_index * rows + jnp.arange(rows, dtype=jnp.int32)
    segment, positions = segment_info(lengths, local_index)
    local_heads = queries.shape[1] // HD
    partial_value = jnp.dot(tokens, kv_weight, preferred_element_type=jnp.float32)
    heads_here = partial_value.shape[1] // (2 * HD)
    per_head = tp_size // heads_here
    pieces = partial_value.astype(jnp.bfloat16).reshape(rows, heads_here, 2 * HD)
    pieces = jnp.repeat(jnp.transpose(pieces, (1, 0, 2)), per_head, axis=0)
    arrived = lax.all_to_all(pieces, "tp", 0, 0, tiled=True)
    head_sum = jnp.sum(arrived.astype(jnp.float32), axis=0)
    key_now = rotate(head_sum[:, :HD].reshape(rows, 1, HD), positions).reshape(rows, HD)
    near = jnp.concatenate([key_now, head_sum[:, HD:]], axis=1).astype(jnp.bfloat16)
    mine = lax.dynamic_slice_in_dim(near, (tp_index % per_head) * HD, HD, 1)
    rotated = rotate(queries.astype(jnp.float32).reshape(rows, local_heads, HD), positions).astype(
        jnp.bfloat16
    )
    blocks = []
    for distance in range(BACK, 0, -1):
        blocks.append(shifted(near, "req", distance))
    blocks.append(near)
    window = jnp.concatenate(blocks, axis=0)
    key_total = (BACK + 1) * rows
    key_index = (req_index - BACK) * rows + jnp.arange(key_total, dtype=jnp.int32)
    key_segment, _ = segment_info(lengths, key_index)
    allowed = (
        (key_index[None, :] >= 0)
        & (key_index[None, :] <= local_index[:, None])
        & (key_segment[None, :] == segment[:, None])
    )
    key_head = window[:, :HD]
    value_head = window[:, HD:]
    query_heads = jnp.transpose(rotated, (1, 0, 2))
    scores = lax.dot_general(
        query_heads, key_head, (((2,), (1,)), ((), ())), preferred_element_type=jnp.float32
    ) / math.sqrt(HD)
    scores = jnp.where(allowed[None], scores, -1e30)
    largest = jnp.max(scores, axis=2, keepdims=True)
    weights = jnp.exp(scores - largest)
    total = jnp.sum(weights, axis=2, keepdims=True)
    mixed = lax.dot_general(
        weights.astype(jnp.bfloat16), value_head, (((2,), (0,)), ((), ())),
        preferred_element_type=jnp.float32,
    )
    outputs = (mixed / total).astype(jnp.bfloat16)
    attended = jnp.transpose(outputs, (1, 0, 2)).reshape(rows, local_heads * HD)
    share = mine.shape[1]
    pages_here = page_owner.shape[0]
    owners = page_owner[:, 0]
    page_rows = rows // pages_here
    capacity = 2 * pages_here // lax.axis_size("req")
    order = jnp.arange(pages_here, dtype=jnp.int32)
    earlier = (owners[:, None] == owners[None, :]) & (order[None, :] < order[:, None])
    rank = jnp.sum(earlier.astype(jnp.int32), axis=1)
    target = owners * capacity + rank
    slots = lax.axis_size("req") * capacity
    placing = (jnp.arange(slots, dtype=jnp.int32)[:, None] == target[None, :]).astype(jnp.bfloat16)
    paged = mine.reshape(pages_here, page_rows * share)
    outgoing = jnp.dot(placing, paged, preferred_element_type=jnp.float32).astype(jnp.bfloat16)
    incoming = lax.all_to_all(outgoing, "req", split_axis=0, concat_axis=0, tiled=True)
    cache = incoming.reshape(slots * page_rows, share)
    return (attended, cache)


def solution(mesh):
    in_specs = (P("req", "tp"), P("tp", None), P("req", "tp"), P(), P("req", None))
    out_specs = (P("req", "tp"), P("req", "tp"))
    return jax.shard_map(layer, mesh=mesh, in_specs=in_specs, out_specs=out_specs, check_vma=False)
```

```python
import math

import jax
import jax.numpy as jnp
from jax import lax
from jax.sharding import PartitionSpec as P


HD = 128
BACK = 3


rope_base = 500000.0


def shifted(value, axis, steps):
    count = lax.axis_size(axis)
    first, last = (max(0, -steps), min(count, count - steps))
    return lax.ppermute(value, axis, [(source, source + steps) for source in range(first, last)])


def rotate(values, positions):
    middle = HD // 2
    frequency = rope_base ** (-(2.0 * jnp.arange(middle, dtype=jnp.float32)) / HD)
    angles = positions.astype(jnp.float32)[:, None] * frequency[None, :]
    cosine = jnp.cos(angles)[:, None, :]
    sine = jnp.sin(angles)[:, None, :]
    front = values[..., :middle]
    behind = values[..., middle:]
    return jnp.concatenate(
        [front * cosine - behind * sine, behind * cosine + front * sine], axis=-1
    )


def segment_info(lengths, indices):
    ends = jnp.cumsum(lengths)
    before = ends[None, :] <= indices[:, None]
    segment = jnp.sum(before.astype(jnp.int32), axis=1)
    start = jnp.sum(jnp.where(before, lengths[None, :], 0), axis=1)
    return (segment, indices - start)


def layer(tokens, kv_weight, queries, lengths, page_owner):
    rows = tokens.shape[0]
    tp_size = lax.axis_size("tp")
    tp_index = lax.axis_index("tp")
    req_index = lax.axis_index("req")
    local_index = req_index * rows + jnp.arange(rows, dtype=jnp.int32)
    segment, positions = segment_info(lengths, local_index)
    local_heads = queries.shape[1] // HD
    partial_value = jnp.dot(tokens, kv_weight, preferred_element_type=jnp.float32)
    pieces = partial_value.astype(jnp.bfloat16).reshape(rows, tp_size, HD)
    arrived = lax.all_to_all(jnp.transpose(pieces, (1, 0, 2)), "tp", 0, 0, tiled=True)
    own = jnp.sum(arrived.astype(jnp.float32), axis=0)
    is_key = tp_index % 2 == 0
    turned = rotate(own.reshape(rows, 1, HD), positions).reshape(rows, HD)
    mine = jnp.where(is_key, turned, own).astype(jnp.bfloat16)
    other = lax.ppermute(mine, "tp", [(i, i ^ 1) for i in range(tp_size)])
    near = jnp.concatenate([jnp.where(is_key, mine, other), jnp.where(is_key, other, mine)], axis=1)
    rotated = rotate(queries.astype(jnp.float32).reshape(rows, local_heads, HD), positions).astype(
        jnp.bfloat16
    )
    blocks = []
    for distance in range(BACK, 0, -1):
        blocks.append(shifted(near, "req", distance))
    blocks.append(near)
    window = jnp.concatenate(blocks, axis=0)
    key_total = (BACK + 1) * rows
    key_index = (req_index - BACK) * rows + jnp.arange(key_total, dtype=jnp.int32)
    key_segment, _ = segment_info(lengths, key_index)
    allowed = (
        (key_index[None, :] >= 0)
        & (key_index[None, :] <= local_index[:, None])
        & (key_segment[None, :] == segment[:, None])
    )
    key_head = window[:, :HD]
    value_head = window[:, HD:]
    query_heads = jnp.transpose(rotated, (1, 0, 2))
    scores = lax.dot_general(
        query_heads, key_head, (((2,), (1,)), ((), ())), preferred_element_type=jnp.float32
    ) / math.sqrt(HD)
    scores = jnp.where(allowed[None], scores, -1e30)
    largest = jnp.max(scores, axis=2, keepdims=True)
    weights = jnp.exp(scores - largest)
    total = jnp.sum(weights, axis=2, keepdims=True)
    mixed = lax.dot_general(
        weights.astype(jnp.bfloat16), value_head, (((2,), (0,)), ((), ())),
        preferred_element_type=jnp.float32,
    )
    outputs = (mixed / total).astype(jnp.bfloat16)
    attended = jnp.transpose(outputs, (1, 0, 2)).reshape(rows, local_heads * HD)
    share = mine.shape[1]
    pages_here = page_owner.shape[0]
    owners = page_owner[:, 0]
    page_rows = rows // pages_here
    capacity = 2 * pages_here // lax.axis_size("req")
    order = jnp.arange(pages_here, dtype=jnp.int32)
    earlier = (owners[:, None] == owners[None, :]) & (order[None, :] < order[:, None])
    rank = jnp.sum(earlier.astype(jnp.int32), axis=1)
    target = owners * capacity + rank
    slots = lax.axis_size("req") * capacity
    placing = (jnp.arange(slots, dtype=jnp.int32)[:, None] == target[None, :]).astype(jnp.bfloat16)
    paged = mine.reshape(pages_here, page_rows * share)
    outgoing = jnp.dot(placing, paged, preferred_element_type=jnp.float32).astype(jnp.bfloat16)
    incoming = lax.all_to_all(outgoing, "req", split_axis=0, concat_axis=0, tiled=True)
    cache = incoming.reshape(slots * page_rows, share)
    return (attended, cache)


def solution(mesh):
    in_specs = (P("req", "tp"), P("tp", None), P("req", "tp"), P(), P("req", None))
    out_specs = (P("req", "tp"), P("req", "tp"))
    return jax.shard_map(layer, mesh=mesh, in_specs=in_specs, out_specs=out_specs, check_vma=False)
```

```python
import math

import jax
import jax.numpy as jnp
from jax import lax
from jax.sharding import PartitionSpec as P


HD = 128
BACK = 3


rope_base = 500000.0


def shifted(value, axis, steps):
    count = lax.axis_size(axis)
    first, last = (max(0, -steps), min(count, count - steps))
    return lax.ppermute(value, axis, [(source, source + steps) for source in range(first, last)])


def rotate(values, positions):
    middle = HD // 2
    frequency = rope_base ** (-(2.0 * jnp.arange(middle, dtype=jnp.float32)) / HD)
    angles = positions.astype(jnp.float32)[:, None] * frequency[None, :]
    cosine = jnp.cos(angles)[:, None, :]
    sine = jnp.sin(angles)[:, None, :]
    front = values[..., :middle]
    behind = values[..., middle:]
    return jnp.concatenate(
        [front * cosine - behind * sine, behind * cosine + front * sine], axis=-1
    )


def segment_info(lengths, indices):
    ends = jnp.cumsum(lengths)
    before = ends[None, :] <= indices[:, None]
    segment = jnp.sum(before.astype(jnp.int32), axis=1)
    start = jnp.sum(jnp.where(before, lengths[None, :], 0), axis=1)
    return (segment, indices - start)


def layer(tokens, kv_weight, queries, lengths, page_owner):
    rows = tokens.shape[0]
    tp_size = lax.axis_size("tp")
    tp_index = lax.axis_index("tp")
    req_index = lax.axis_index("req")
    local_index = req_index * rows + jnp.arange(rows, dtype=jnp.int32)
    segment, positions = segment_info(lengths, local_index)
    local_heads = queries.shape[1] // HD
    partial_value = jnp.dot(tokens, kv_weight, preferred_element_type=jnp.float32)
    pieces = partial_value.astype(jnp.bfloat16).reshape(rows, tp_size, HD)
    arrived = lax.all_to_all(jnp.transpose(pieces, (1, 0, 2)), "tp", 0, 0, tiled=True)
    own = jnp.sum(arrived.astype(jnp.float32), axis=0)
    is_key = tp_index % 2 == 0
    turned = rotate(own.reshape(rows, 1, HD), positions).reshape(rows, HD)
    mine = jnp.where(is_key, turned, own).astype(jnp.bfloat16)
    other = lax.ppermute(mine, "tp", [(i, i ^ 1) for i in range(tp_size)])
    near = jnp.concatenate([jnp.where(is_key, mine, other), jnp.where(is_key, other, mine)], axis=1)
    rotated = rotate(queries.astype(jnp.float32).reshape(rows, local_heads, HD), positions).astype(
        jnp.bfloat16
    )
    blocks = []
    for distance in range(BACK, 0, -1):
        blocks.append(shifted(near, "req", distance))
    blocks.append(near)
    window = jnp.concatenate(blocks, axis=0)
    key_total = (BACK + 1) * rows
    key_index = (req_index - BACK) * rows + jnp.arange(key_total, dtype=jnp.int32)
    key_segment, _ = segment_info(lengths, key_index)
    allowed = (
        (key_index[None, :] >= 0)
        & (key_index[None, :] <= local_index[:, None])
        & (key_segment[None, :] == segment[:, None])
    )
    key_head = window[:, :HD]
    value_head = window[:, HD:]
    query_heads = jnp.transpose(rotated, (1, 0, 2))
    scores = lax.dot_general(
        query_heads, key_head, (((2,), (1,)), ((), ())), preferred_element_type=jnp.float32
    ) / math.sqrt(HD)
    scores = jnp.where(allowed[None], scores, -1e30)
    largest = jnp.max(scores, axis=2, keepdims=True)
    weights = jnp.exp(scores - largest)
    total = jnp.sum(weights, axis=2, keepdims=True)
    mixed = lax.dot_general(
        weights.astype(jnp.bfloat16), value_head, (((2,), (0,)), ((), ())),
        preferred_element_type=jnp.float32,
    )
    outputs = (mixed / total).astype(jnp.bfloat16)
    attended = jnp.transpose(outputs, (1, 0, 2)).reshape(rows, local_heads * HD)
    share = mine.shape[1]
    pages_here = page_owner.shape[0]
    owners = page_owner[:, 0]
    page_rows = rows // pages_here
    capacity = 2 * pages_here // lax.axis_size("req")
    order = jnp.arange(pages_here, dtype=jnp.int32)
    earlier = (owners[:, None] == owners[None, :]) & (order[None, :] < order[:, None])
    rank = jnp.sum(earlier.astype(jnp.int32), axis=1)
    count = lax.axis_size("req")
    side = math.isqrt(count)
    assert side * side == count
    target = (owners % side) * (side * capacity) + (owners // side) * capacity + rank
    slots = count * capacity
    placing = (jnp.arange(slots, dtype=jnp.int32)[:, None] == target[None, :]).astype(jnp.bfloat16)
    paged = mine.reshape(pages_here, page_rows * share)
    outgoing = jnp.dot(placing, paged, preferred_element_type=jnp.float32).astype(jnp.bfloat16)
    lows = [[side * a + b for b in range(side)] for a in range(side)]
    highs = [[side * a + b for a in range(side)] for b in range(side)]
    middle = lax.all_to_all(outgoing, "req", 0, 0, tiled=True, axis_index_groups=lows)
    middle = jnp.transpose(middle.reshape(side, side, capacity, -1), (1, 0, 2, 3)).reshape(slots, -1)
    incoming = lax.all_to_all(middle, "req", 0, 0, tiled=True, axis_index_groups=highs)
    cache = incoming.reshape(slots * page_rows, share)
    return (attended, cache)


def solution(mesh):
    in_specs = (P("req", "tp"), P("tp", None), P("req", "tp"), P(), P("req", None))
    out_specs = (P("req", "tp"), P("req", "tp"))
    return jax.shard_map(layer, mesh=mesh, in_specs=in_specs, out_specs=out_specs, check_vma=False)
```

```python
import math

import jax
import jax.numpy as jnp
from jax import lax
from jax.sharding import PartitionSpec as P


HD = 128
BACK = 3


rope_base = 500000.0


def shifted(value, axis, steps):
    count = lax.axis_size(axis)
    first, last = (max(0, -steps), min(count, count - steps))
    return lax.ppermute(value, axis, [(source, source + steps) for source in range(first, last)])


def rotate(values, positions):
    middle = HD // 2
    frequency = rope_base ** (-(2.0 * jnp.arange(middle, dtype=jnp.float32)) / HD)
    angles = positions.astype(jnp.float32)[:, None] * frequency[None, :]
    cosine = jnp.cos(angles)[:, None, :]
    sine = jnp.sin(angles)[:, None, :]
    front = values[..., :middle]
    behind = values[..., middle:]
    return jnp.concatenate(
        [front * cosine - behind * sine, behind * cosine + front * sine], axis=-1
    )


def segment_info(lengths, indices):
    ends = jnp.cumsum(lengths)
    before = ends[None, :] <= indices[:, None]
    segment = jnp.sum(before.astype(jnp.int32), axis=1)
    start = jnp.sum(jnp.where(before, lengths[None, :], 0), axis=1)
    return (segment, indices - start)


def layer(tokens, kv_weight, queries, lengths, page_owner):
    rows = tokens.shape[0]
    tp_size = lax.axis_size("tp")
    tp_index = lax.axis_index("tp")
    req_index = lax.axis_index("req")
    local_index = req_index * rows + jnp.arange(rows, dtype=jnp.int32)
    segment, positions = segment_info(lengths, local_index)
    local_heads = queries.shape[1] // HD
    partial_value = jnp.dot(tokens, kv_weight, preferred_element_type=jnp.float32)
    pieces = partial_value.astype(jnp.bfloat16).reshape(rows, tp_size, HD)
    arrived = lax.all_to_all(jnp.transpose(pieces, (1, 0, 2)), "tp", 0, 0, tiled=True)
    own = jnp.sum(arrived.astype(jnp.float32), axis=0)
    is_key = tp_index % 2 == 0
    turned = rotate(own.reshape(rows, 1, HD), positions).reshape(rows, HD)
    mine = jnp.where(is_key, turned, own).astype(jnp.bfloat16)
    other = lax.ppermute(mine, "tp", [(i, i ^ 1) for i in range(tp_size)])
    near = jnp.concatenate([jnp.where(is_key, mine, other), jnp.where(is_key, other, mine)], axis=1)
    rotated = rotate(queries.astype(jnp.float32).reshape(rows, local_heads, HD), positions).astype(
        jnp.bfloat16
    )
    blocks = []
    for distance in range(BACK, 0, -1):
        blocks.append(shifted(near, "req", distance))
    blocks.append(near)
    window = jnp.concatenate(blocks, axis=0)
    key_total = (BACK + 1) * rows
    key_index = (req_index - BACK) * rows + jnp.arange(key_total, dtype=jnp.int32)
    key_segment, _ = segment_info(lengths, key_index)
    allowed = (
        (key_index[None, :] >= 0)
        & (key_index[None, :] <= local_index[:, None])
        & (key_segment[None, :] == segment[:, None])
    )
    key_head = window[:, :HD]
    value_head = window[:, HD:]
    scores = lax.dot_general(
        rotated, key_head, (((2,), (1,)), ((), ())), preferred_element_type=jnp.float32
    ) / math.sqrt(HD)
    scores = jnp.where(allowed[:, None, :], scores, -1e30)
    largest = jnp.max(scores, axis=2, keepdims=True)
    weights = jnp.exp(scores - largest)
    total = jnp.sum(weights, axis=2, keepdims=True)
    mixed = lax.dot_general(
        weights.astype(jnp.bfloat16), value_head, (((2,), (0,)), ((), ())),
        preferred_element_type=jnp.float32,
    )
    attended = (mixed / total).astype(jnp.bfloat16).reshape(rows, local_heads * HD)
    pages_here = page_owner.shape[0]
    owners = page_owner[:, 0]
    page_rows = rows // pages_here
    capacity = 2 * pages_here // lax.axis_size("req")
    order = jnp.arange(pages_here, dtype=jnp.int32)
    earlier = (owners[:, None] == owners[None, :]) & (order[None, :] < order[:, None])
    rank = jnp.sum(earlier.astype(jnp.int32), axis=1)
    target = owners * capacity + rank
    slots = lax.axis_size("req") * capacity
    row_target = (target[:, None] * page_rows + jnp.arange(page_rows, dtype=jnp.int32)[None, :]).reshape(rows)
    placing = (jnp.arange(slots * page_rows, dtype=jnp.int32)[:, None] == row_target[None, :]).astype(jnp.bfloat16)
    outgoing = jnp.dot(placing, mine, preferred_element_type=jnp.float32).astype(jnp.bfloat16)
    cache = lax.all_to_all(outgoing, "req", 0, 0, tiled=True)
    return (attended, cache)


def solution(mesh):
    in_specs = (P("req", "tp"), P("tp", None), P("req", "tp"), P(), P("req", None))
    out_specs = (P("req", "tp"), P("req", "tp"))
    return jax.shard_map(layer, mesh=mesh, in_specs=in_specs, out_specs=out_specs, check_vma=False)
```

```python
import math

import jax
import jax.numpy as jnp
from jax import lax
from jax.experimental import pallas as pl
from jax.sharding import PartitionSpec as P


HD = 128
BACK = 3


rope_base = 500000.0


def shifted(value, axis, steps):
    count = lax.axis_size(axis)
    first, last = (max(0, -steps), min(count, count - steps))
    return lax.ppermute(value, axis, [(source, source + steps) for source in range(first, last)])


def rotate(values, positions):
    middle = HD // 2
    frequency = rope_base ** (-(2.0 * jnp.arange(middle, dtype=jnp.float32)) / HD)
    angles = positions.astype(jnp.float32)[:, None] * frequency[None, :]
    cosine = jnp.cos(angles)[:, None, :]
    sine = jnp.sin(angles)[:, None, :]
    front = values[..., :middle]
    behind = values[..., middle:]
    return jnp.concatenate(
        [front * cosine - behind * sine, behind * cosine + front * sine], axis=-1
    )


def project_kernel(tokens_ref, weight_ref, out_ref):
    product = jnp.dot(tokens_ref[...], weight_ref[...], preferred_element_type=jnp.float32)
    for block in range(out_ref.shape[0]):
        out_ref[block] = product[:, block * HD : (block + 1) * HD].astype(out_ref.dtype)


def project(tokens, kv_weight, per_step=2):
    rows, features = tokens.shape
    blocks = kv_weight.shape[1] // HD
    return pl.pallas_call(
        project_kernel,
        grid=(blocks // per_step,),
        in_specs=[
            pl.BlockSpec((rows, features), lambda j: (0, 0)),
            pl.BlockSpec((features, per_step * HD), lambda j: (0, j)),
        ],
        out_specs=pl.BlockSpec((per_step, rows, HD), lambda j: (j, 0, 0)),
        out_shape=jax.ShapeDtypeStruct((blocks, rows, HD), jnp.bfloat16),
    )(tokens, kv_weight)


def segment_info(lengths, indices):
    ends = jnp.cumsum(lengths)
    before = ends[None, :] <= indices[:, None]
    segment = jnp.sum(before.astype(jnp.int32), axis=1)
    start = jnp.sum(jnp.where(before, lengths[None, :], 0), axis=1)
    return (segment, indices - start)


def layer(tokens, kv_weight, queries, lengths, page_owner):
    rows = tokens.shape[0]
    tp_size = lax.axis_size("tp")
    tp_index = lax.axis_index("tp")
    req_index = lax.axis_index("req")
    local_index = req_index * rows + jnp.arange(rows, dtype=jnp.int32)
    segment, positions = segment_info(lengths, local_index)
    local_heads = queries.shape[1] // HD
    pieces = project(tokens, kv_weight)
    arrived = lax.all_to_all(pieces, "tp", 0, 0, tiled=True)
    own = jnp.sum(arrived.astype(jnp.float32), axis=0)
    is_key = tp_index % 2 == 0
    turned = rotate(own.reshape(rows, 1, HD), positions).reshape(rows, HD)
    mine = jnp.where(is_key, turned, own).astype(jnp.bfloat16)
    other = lax.ppermute(mine, "tp", [(i, i ^ 1) for i in range(tp_size)])
    near = jnp.concatenate([jnp.where(is_key, mine, other), jnp.where(is_key, other, mine)], axis=1)
    rotated = rotate(queries.astype(jnp.float32).reshape(rows, local_heads, HD), positions).astype(
        jnp.bfloat16
    )
    blocks = []
    for distance in range(BACK, 0, -1):
        blocks.append(shifted(near, "req", distance))
    blocks.append(near)
    window = jnp.concatenate(blocks, axis=0)
    key_total = (BACK + 1) * rows
    key_index = (req_index - BACK) * rows + jnp.arange(key_total, dtype=jnp.int32)
    key_segment, _ = segment_info(lengths, key_index)
    allowed = (
        (key_index[None, :] >= 0)
        & (key_index[None, :] <= local_index[:, None])
        & (key_segment[None, :] == segment[:, None])
    )
    key_head = window[:, :HD]
    value_head = window[:, HD:]
    scores = lax.dot_general(
        rotated, key_head, (((2,), (1,)), ((), ())), preferred_element_type=jnp.float32
    ) / math.sqrt(HD)
    scores = jnp.where(allowed[:, None, :], scores, -1e30)
    largest = jnp.max(scores, axis=2, keepdims=True)
    weights = jnp.exp(scores - largest)
    total = jnp.sum(weights, axis=2, keepdims=True)
    mixed = lax.dot_general(
        weights.astype(jnp.bfloat16), value_head, (((2,), (0,)), ((), ())),
        preferred_element_type=jnp.float32,
    )
    attended = (mixed / total).astype(jnp.bfloat16).reshape(rows, local_heads * HD)
    pages_here = page_owner.shape[0]
    owners = page_owner[:, 0]
    page_rows = rows // pages_here
    capacity = 2 * pages_here // lax.axis_size("req")
    order = jnp.arange(pages_here, dtype=jnp.int32)
    earlier = (owners[:, None] == owners[None, :]) & (order[None, :] < order[:, None])
    rank = jnp.sum(earlier.astype(jnp.int32), axis=1)
    target = owners * capacity + rank
    slots = lax.axis_size("req") * capacity
    row_target = (target[:, None] * page_rows + jnp.arange(page_rows, dtype=jnp.int32)[None, :]).reshape(rows)
    placing = (jnp.arange(slots * page_rows, dtype=jnp.int32)[:, None] == row_target[None, :]).astype(jnp.bfloat16)
    outgoing = jnp.dot(placing, mine, preferred_element_type=jnp.float32).astype(jnp.bfloat16)
    cache = lax.all_to_all(outgoing, "req", 0, 0, tiled=True)
    return (attended, cache)


def solution(mesh):
    in_specs = (P("req", "tp"), P("tp", None), P("req", "tp"), P(), P("req", None))
    out_specs = (P("req", "tp"), P("req", "tp"))
    return jax.shard_map(layer, mesh=mesh, in_specs=in_specs, out_specs=out_specs, check_vma=False)
```

```python
import math

import jax
import jax.numpy as jnp
from jax import lax
from jax.sharding import PartitionSpec as P


HD = 128
BACK = 3


rope_base = 500000.0


def shifted(value, axis, steps):
    count = lax.axis_size(axis)
    first, last = (max(0, -steps), min(count, count - steps))
    return lax.ppermute(value, axis, [(source, source + steps) for source in range(first, last)])


def rotate(values, positions):
    middle = HD // 2
    frequency = rope_base ** (-(2.0 * jnp.arange(middle, dtype=jnp.float32)) / HD)
    angles = positions.astype(jnp.float32)[:, None] * frequency[None, :]
    cosine = jnp.cos(angles)[:, None, :]
    sine = jnp.sin(angles)[:, None, :]
    front = values[..., :middle]
    behind = values[..., middle:]
    return jnp.concatenate(
        [front * cosine - behind * sine, behind * cosine + front * sine], axis=-1
    )


def segment_info(lengths, indices):
    ends = jnp.cumsum(lengths)
    before = ends[None, :] <= indices[:, None]
    segment = jnp.sum(before.astype(jnp.int32), axis=1)
    start = jnp.sum(jnp.where(before, lengths[None, :], 0), axis=1)
    return (segment, indices - start)


def layer(tokens, kv_weight, queries, lengths, page_owner):
    rows = tokens.shape[0]
    tp_size = lax.axis_size("tp")
    tp_index = lax.axis_index("tp")
    req_index = lax.axis_index("req")
    local_index = req_index * rows + jnp.arange(rows, dtype=jnp.int32)
    segment, positions = segment_info(lengths, local_index)
    local_heads = queries.shape[1] // HD
    partial_value = jnp.dot(tokens, kv_weight, preferred_element_type=jnp.float32)
    heads_here = partial_value.shape[1] // (2 * HD)
    per_head = tp_size // heads_here
    half = rows // per_head
    parts = partial_value.reshape(rows, heads_here, 2, HD)
    key_high = lax.optimization_barrier(parts[:, :, 0, :].astype(jnp.bfloat16))
    key_low = (parts[:, :, 0, :] - key_high.astype(jnp.float32)).astype(jnp.bfloat16)
    value_high = parts[:, :, 1, :].astype(jnp.bfloat16)
    packed = jnp.concatenate([key_high, key_low, value_high], axis=2)
    packed = jnp.transpose(packed.reshape(per_head, half, heads_here, 3 * HD), (2, 0, 1, 3))
    arrived = lax.all_to_all(packed.reshape(tp_size, half, 3 * HD), "tp", 0, 0, tiled=True)
    arrived = jnp.sum(arrived.astype(jnp.float32), axis=0)
    side = tp_index % per_head
    key_sum = arrived[:, :HD] + arrived[:, HD : 2 * HD]
    here = lax.dynamic_slice_in_dim(positions, side * half, half, 0)
    key_now = rotate(key_sum.reshape(half, 1, HD), here).reshape(half, HD)
    finished = jnp.concatenate([key_now, arrived[:, 2 * HD :]], axis=1).astype(jnp.bfloat16)
    other = lax.ppermute(finished, "tp", [(i, i ^ 1) for i in range(tp_size)])
    first = side == 0
    near = jnp.concatenate([jnp.where(first, finished, other), jnp.where(first, other, finished)], axis=0)
    mine = lax.dynamic_slice_in_dim(near, side * HD, HD, 1)
    rotated = rotate(queries.astype(jnp.float32).reshape(rows, local_heads, HD), positions).astype(
        jnp.bfloat16
    )
    blocks = []
    for distance in range(BACK, 0, -1):
        blocks.append(shifted(near, "req", distance))
    blocks.append(near)
    window = jnp.concatenate(blocks, axis=0)
    key_total = (BACK + 1) * rows
    key_index = (req_index - BACK) * rows + jnp.arange(key_total, dtype=jnp.int32)
    key_segment, _ = segment_info(lengths, key_index)
    allowed = (
        (key_index[None, :] >= 0)
        & (key_index[None, :] <= local_index[:, None])
        & (key_segment[None, :] == segment[:, None])
    )
    key_head = window[:, :HD]
    value_head = window[:, HD:]
    scores = lax.dot_general(
        rotated, key_head, (((2,), (1,)), ((), ())), preferred_element_type=jnp.float32
    ) / math.sqrt(HD)
    scores = jnp.where(allowed[:, None, :], scores, -1e30)
    largest = jnp.max(scores, axis=2, keepdims=True)
    weights = jnp.exp(scores - largest)
    total = jnp.sum(weights, axis=2, keepdims=True)
    mixed = lax.dot_general(
        weights.astype(jnp.bfloat16), value_head, (((2,), (0,)), ((), ())),
        preferred_element_type=jnp.float32,
    )
    attended = (mixed / total).astype(jnp.bfloat16).reshape(rows, local_heads * HD)
    pages_here = page_owner.shape[0]
    owners = page_owner[:, 0]
    page_rows = rows // pages_here
    capacity = 2 * pages_here // lax.axis_size("req")
    order = jnp.arange(pages_here, dtype=jnp.int32)
    earlier = (owners[:, None] == owners[None, :]) & (order[None, :] < order[:, None])
    rank = jnp.sum(earlier.astype(jnp.int32), axis=1)
    target = owners * capacity + rank
    slots = lax.axis_size("req") * capacity
    row_target = (target[:, None] * page_rows + jnp.arange(page_rows, dtype=jnp.int32)[None, :]).reshape(rows)
    placing = (jnp.arange(slots * page_rows, dtype=jnp.int32)[:, None] == row_target[None, :]).astype(jnp.bfloat16)
    outgoing = jnp.dot(placing, mine, preferred_element_type=jnp.float32).astype(jnp.bfloat16)
    cache = lax.all_to_all(outgoing, "req", 0, 0, tiled=True)
    return (attended, cache)


def solution(mesh):
    in_specs = (P("req", "tp"), P("tp", None), P("req", "tp"), P(), P("req", None))
    out_specs = (P("req", "tp"), P("req", "tp"))
    return jax.shard_map(layer, mesh=mesh, in_specs=in_specs, out_specs=out_specs, check_vma=False)
```

```python
import math

import jax
import jax.numpy as jnp
from jax import lax
from jax.sharding import PartitionSpec as P


HD = 128
BACK = 3


rope_base = 500000.0


def shifted(value, axis, steps):
    count = lax.axis_size(axis)
    first, last = (max(0, -steps), min(count, count - steps))
    return lax.ppermute(value, axis, [(source, source + steps) for source in range(first, last)])


def rotate(values, positions):
    middle = HD // 2
    frequency = rope_base ** (-(2.0 * jnp.arange(middle, dtype=jnp.float32)) / HD)
    angles = positions.astype(jnp.float32)[:, None] * frequency[None, :]
    cosine = jnp.cos(angles)[:, None, :]
    sine = jnp.sin(angles)[:, None, :]
    front = values[..., :middle]
    behind = values[..., middle:]
    return jnp.concatenate(
        [front * cosine - behind * sine, behind * cosine + front * sine], axis=-1
    )


def segment_info(lengths, indices):
    ends = jnp.cumsum(lengths)
    before = ends[None, :] <= indices[:, None]
    segment = jnp.sum(before.astype(jnp.int32), axis=1)
    start = jnp.sum(jnp.where(before, lengths[None, :], 0), axis=1)
    return (segment, indices - start)


def layer(tokens, kv_weight, queries, lengths, page_owner):
    rows = tokens.shape[0]
    tp_size = lax.axis_size("tp")
    tp_index = lax.axis_index("tp")
    req_index = lax.axis_index("req")
    local_index = req_index * rows + jnp.arange(rows, dtype=jnp.int32)
    segment, positions = segment_info(lengths, local_index)
    local_heads = queries.shape[1] // HD
    partial_value = jnp.dot(tokens, kv_weight, preferred_element_type=jnp.float32)
    heads_here = partial_value.shape[1] // (2 * HD)
    per_head = tp_size // heads_here
    half = rows // per_head
    high = lax.optimization_barrier(partial_value.astype(jnp.bfloat16))
    low = (partial_value - high.astype(jnp.float32)).astype(jnp.bfloat16)
    chunks = []
    for head in range(heads_here):
        for part in range(per_head):
            lines = slice(part * half, (part + 1) * half)
            chunks.append(jnp.concatenate([
                high[lines, head * 2 * HD : (head + 1) * 2 * HD],
                low[lines, head * 2 * HD : head * 2 * HD + HD],
            ], axis=1))
    arrived = lax.all_to_all(jnp.stack(chunks), "tp", 0, 0, tiled=True)
    arrived = jnp.sum(arrived.astype(jnp.float32), axis=0)
    side = tp_index % per_head
    key_sum = arrived[:, :HD] + arrived[:, 2 * HD :]
    here = lax.dynamic_slice_in_dim(positions, side * half, half, 0)
    key_now = rotate(key_sum.reshape(half, 1, HD), here).reshape(half, HD)
    finished = jnp.concatenate([key_now, arrived[:, HD : 2 * HD]], axis=1).astype(jnp.bfloat16)
    other = lax.ppermute(finished, "tp", [(i, i ^ 1) for i in range(tp_size)])
    first = side == 0
    near = jnp.concatenate([jnp.where(first, finished, other), jnp.where(first, other, finished)], axis=0)
    mine = lax.dynamic_slice_in_dim(near, side * HD, HD, 1)
    rotated = rotate(queries.astype(jnp.float32).reshape(rows, local_heads, HD), positions).astype(
        jnp.bfloat16
    )
    blocks = []
    for distance in range(BACK, 0, -1):
        blocks.append(shifted(near, "req", distance))
    blocks.append(near)
    window = jnp.concatenate(blocks, axis=0)
    key_total = (BACK + 1) * rows
    key_index = (req_index - BACK) * rows + jnp.arange(key_total, dtype=jnp.int32)
    key_segment, _ = segment_info(lengths, key_index)
    allowed = (
        (key_index[None, :] >= 0)
        & (key_index[None, :] <= local_index[:, None])
        & (key_segment[None, :] == segment[:, None])
    )
    key_head = window[:, :HD]
    value_head = window[:, HD:]
    scores = lax.dot_general(
        rotated, key_head, (((2,), (1,)), ((), ())), preferred_element_type=jnp.float32
    ) / math.sqrt(HD)
    scores = jnp.where(allowed[:, None, :], scores, -1e30)
    largest = jnp.max(scores, axis=2, keepdims=True)
    weights = jnp.exp(scores - largest)
    total = jnp.sum(weights, axis=2, keepdims=True)
    mixed = lax.dot_general(
        weights.astype(jnp.bfloat16), value_head, (((2,), (0,)), ((), ())),
        preferred_element_type=jnp.float32,
    )
    attended = (mixed / total).astype(jnp.bfloat16).reshape(rows, local_heads * HD)
    pages_here = page_owner.shape[0]
    owners = page_owner[:, 0]
    page_rows = rows // pages_here
    capacity = 2 * pages_here // lax.axis_size("req")
    order = jnp.arange(pages_here, dtype=jnp.int32)
    earlier = (owners[:, None] == owners[None, :]) & (order[None, :] < order[:, None])
    rank = jnp.sum(earlier.astype(jnp.int32), axis=1)
    target = owners * capacity + rank
    slots = lax.axis_size("req") * capacity
    row_target = (target[:, None] * page_rows + jnp.arange(page_rows, dtype=jnp.int32)[None, :]).reshape(rows)
    placing = (jnp.arange(slots * page_rows, dtype=jnp.int32)[:, None] == row_target[None, :]).astype(jnp.bfloat16)
    outgoing = jnp.dot(placing, mine, preferred_element_type=jnp.float32).astype(jnp.bfloat16)
    cache = lax.all_to_all(outgoing, "req", 0, 0, tiled=True)
    return (attended, cache)


def solution(mesh):
    in_specs = (P("req", "tp"), P("tp", None), P("req", "tp"), P(), P("req", None))
    out_specs = (P("req", "tp"), P("req", "tp"))
    return jax.shard_map(layer, mesh=mesh, in_specs=in_specs, out_specs=out_specs, check_vma=False)
```

```python
import math

import jax
import jax.numpy as jnp
from jax import lax
from jax.sharding import PartitionSpec as P


HD = 128
BACK = 3


rope_base = 500000.0


def shifted(value, axis, steps):
    count = lax.axis_size(axis)
    first, last = (max(0, -steps), min(count, count - steps))
    return lax.ppermute(value, axis, [(source, source + steps) for source in range(first, last)])


def rotate(values, positions):
    middle = HD // 2
    frequency = rope_base ** (-(2.0 * jnp.arange(middle, dtype=jnp.float32)) / HD)
    angles = positions.astype(jnp.float32)[:, None] * frequency[None, :]
    cosine = jnp.cos(angles)[:, None, :]
    sine = jnp.sin(angles)[:, None, :]
    front = values[..., :middle]
    behind = values[..., middle:]
    return jnp.concatenate(
        [front * cosine - behind * sine, behind * cosine + front * sine], axis=-1
    )


def segment_info(lengths, indices):
    ends = jnp.cumsum(lengths)
    before = ends[None, :] <= indices[:, None]
    segment = jnp.sum(before.astype(jnp.int32), axis=1)
    start = jnp.sum(jnp.where(before, lengths[None, :], 0), axis=1)
    return (segment, indices - start)


def layer(tokens, kv_weight, queries, lengths, page_owner):
    rows = tokens.shape[0]
    tp_size = lax.axis_size("tp")
    tp_index = lax.axis_index("tp")
    req_index = lax.axis_index("req")
    local_index = req_index * rows + jnp.arange(rows, dtype=jnp.int32)
    segment, positions = segment_info(lengths, local_index)
    local_heads = queries.shape[1] // HD
    pieces = jnp.stack([
        jnp.dot(tokens, kv_weight[:, block * HD : (block + 1) * HD], preferred_element_type=jnp.float32)
        for block in range(tp_size)
    ])
    arrived = lax.all_to_all(pieces, "tp", 0, 0, tiled=True)
    own = jnp.sum(arrived, axis=0)
    is_key = tp_index % 2 == 0
    turned = rotate(own.reshape(rows, 1, HD), positions).reshape(rows, HD)
    mine = jnp.where(is_key, turned, own).astype(jnp.bfloat16)
    other = lax.ppermute(mine, "tp", [(i, i ^ 1) for i in range(tp_size)])
    near = jnp.concatenate([jnp.where(is_key, mine, other), jnp.where(is_key, other, mine)], axis=1)
    rotated = rotate(queries.astype(jnp.float32).reshape(rows, local_heads, HD), positions).astype(
        jnp.bfloat16
    )
    blocks = []
    for distance in range(BACK, 0, -1):
        blocks.append(shifted(near, "req", distance))
    blocks.append(near)
    window = jnp.concatenate(blocks, axis=0)
    key_total = (BACK + 1) * rows
    key_index = (req_index - BACK) * rows + jnp.arange(key_total, dtype=jnp.int32)
    key_segment, _ = segment_info(lengths, key_index)
    allowed = (
        (key_index[None, :] >= 0)
        & (key_index[None, :] <= local_index[:, None])
        & (key_segment[None, :] == segment[:, None])
    )
    key_head = window[:, :HD]
    value_head = window[:, HD:]
    scores = lax.dot_general(
        rotated, key_head, (((2,), (1,)), ((), ())), preferred_element_type=jnp.float32
    ) / math.sqrt(HD)
    scores = jnp.where(allowed[:, None, :], scores, -1e30)
    largest = jnp.max(scores, axis=2, keepdims=True)
    weights = jnp.exp(scores - largest)
    total = jnp.sum(weights, axis=2, keepdims=True)
    mixed = lax.dot_general(
        weights.astype(jnp.bfloat16), value_head, (((2,), (0,)), ((), ())),
        preferred_element_type=jnp.float32,
    )
    attended = (mixed / total).astype(jnp.bfloat16).reshape(rows, local_heads * HD)
    pages_here = page_owner.shape[0]
    owners = page_owner[:, 0]
    page_rows = rows // pages_here
    capacity = 2 * pages_here // lax.axis_size("req")
    order = jnp.arange(pages_here, dtype=jnp.int32)
    earlier = (owners[:, None] == owners[None, :]) & (order[None, :] < order[:, None])
    rank = jnp.sum(earlier.astype(jnp.int32), axis=1)
    target = owners * capacity + rank
    slots = lax.axis_size("req") * capacity
    row_target = (target[:, None] * page_rows + jnp.arange(page_rows, dtype=jnp.int32)[None, :]).reshape(rows)
    placing = (jnp.arange(slots * page_rows, dtype=jnp.int32)[:, None] == row_target[None, :]).astype(jnp.bfloat16)
    outgoing = jnp.dot(placing, mine, preferred_element_type=jnp.float32).astype(jnp.bfloat16)
    cache = lax.all_to_all(outgoing, "req", 0, 0, tiled=True)
    return (attended, cache)


def solution(mesh):
    in_specs = (P("req", "tp"), P("tp", None), P("req", "tp"), P(), P("req", None))
    out_specs = (P("req", "tp"), P("req", "tp"))
    return jax.shard_map(layer, mesh=mesh, in_specs=in_specs, out_specs=out_specs, check_vma=False)
```

```python
import math

import jax
import jax.numpy as jnp
from jax import lax
from jax.sharding import PartitionSpec as P


HD = 128
BACK = 3


rope_base = 500000.0


def shifted(value, axis, steps):
    count = lax.axis_size(axis)
    first, last = (max(0, -steps), min(count, count - steps))
    return lax.ppermute(value, axis, [(source, source + steps) for source in range(first, last)])


def rotate(values, positions):
    middle = HD // 2
    frequency = rope_base ** (-(2.0 * jnp.arange(middle, dtype=jnp.float32)) / HD)
    angles = positions.astype(jnp.float32)[:, None] * frequency[None, :]
    cosine = jnp.cos(angles)[:, None, :]
    sine = jnp.sin(angles)[:, None, :]
    front = values[..., :middle]
    behind = values[..., middle:]
    return jnp.concatenate(
        [front * cosine - behind * sine, behind * cosine + front * sine], axis=-1
    )


def segment_info(lengths, indices):
    ends = jnp.cumsum(lengths)
    before = ends[None, :] <= indices[:, None]
    segment = jnp.sum(before.astype(jnp.int32), axis=1)
    start = jnp.sum(jnp.where(before, lengths[None, :], 0), axis=1)
    return (segment, indices - start)


def layer(tokens, kv_weight, queries, lengths, page_owner):
    rows = tokens.shape[0]
    tp_size = lax.axis_size("tp")
    tp_index = lax.axis_index("tp")
    req_index = lax.axis_index("req")
    local_index = req_index * rows + jnp.arange(rows, dtype=jnp.int32)
    segment, positions = segment_info(lengths, local_index)
    local_heads = queries.shape[1] // HD
    partial_value = jnp.dot(tokens, kv_weight, preferred_element_type=jnp.float32)
    pieces = partial_value.reshape(rows, tp_size, HD)
    arrived = lax.all_to_all(jnp.transpose(pieces, (1, 0, 2)), "tp", 0, 0, tiled=True)
    own = jnp.sum(arrived, axis=0)
    is_key = tp_index % 2 == 0
    turned = rotate(own.reshape(rows, 1, HD), positions).reshape(rows, HD)
    mine = jnp.where(is_key, turned, own).astype(jnp.bfloat16)
    other = lax.ppermute(mine, "tp", [(i, i ^ 1) for i in range(tp_size)])
    near = jnp.concatenate([jnp.where(is_key, mine, other), jnp.where(is_key, other, mine)], axis=1)
    rotated = rotate(queries.astype(jnp.float32).reshape(rows, local_heads, HD), positions).astype(
        jnp.bfloat16
    )
    blocks = []
    for distance in range(BACK, 0, -1):
        blocks.append(shifted(near, "req", distance))
    blocks.append(near)
    window = jnp.concatenate(blocks, axis=0)
    key_total = (BACK + 1) * rows
    key_index = (req_index - BACK) * rows + jnp.arange(key_total, dtype=jnp.int32)
    key_segment, _ = segment_info(lengths, key_index)
    allowed = (
        (key_index[None, :] >= 0)
        & (key_index[None, :] <= local_index[:, None])
        & (key_segment[None, :] == segment[:, None])
    )
    key_head = window[:, :HD]
    value_head = window[:, HD:]
    scores = lax.dot_general(
        rotated, key_head, (((2,), (1,)), ((), ())), preferred_element_type=jnp.float32
    ) / math.sqrt(HD)
    scores = jnp.where(allowed[:, None, :], scores, -1e30)
    largest = jnp.max(scores, axis=2, keepdims=True)
    weights = jnp.exp(scores - largest)
    total = jnp.sum(weights, axis=2, keepdims=True)
    mixed = lax.dot_general(
        weights.astype(jnp.bfloat16), value_head, (((2,), (0,)), ((), ())),
        preferred_element_type=jnp.float32,
    )
    attended = (mixed / total).astype(jnp.bfloat16).reshape(rows, local_heads * HD)
    pages_here = page_owner.shape[0]
    owners = page_owner[:, 0]
    page_rows = rows // pages_here
    capacity = 2 * pages_here // lax.axis_size("req")
    order = jnp.arange(pages_here, dtype=jnp.int32)
    earlier = (owners[:, None] == owners[None, :]) & (order[None, :] < order[:, None])
    rank = jnp.sum(earlier.astype(jnp.int32), axis=1)
    target = owners * capacity + rank
    slots = lax.axis_size("req") * capacity
    row_target = (target[:, None] * page_rows + jnp.arange(page_rows, dtype=jnp.int32)[None, :]).reshape(rows)
    placing = (jnp.arange(slots * page_rows, dtype=jnp.int32)[:, None] == row_target[None, :]).astype(jnp.bfloat16)
    placing = lax.optimization_barrier(placing)
    outgoing = jnp.dot(placing, mine, preferred_element_type=jnp.float32).astype(jnp.bfloat16)
    cache = lax.all_to_all(outgoing, "req", 0, 0, tiled=True)
    return (attended, cache)


def solution(mesh):
    in_specs = (P("req", "tp"), P("tp", None), P("req", "tp"), P(), P("req", None))
    out_specs = (P("req", "tp"), P("req", "tp"))
    return jax.shard_map(layer, mesh=mesh, in_specs=in_specs, out_specs=out_specs, check_vma=False)
```

```python
import math

import jax
import jax.numpy as jnp
from jax import lax
from jax.sharding import PartitionSpec as P


HD = 128
BACK = 3


rope_base = 500000.0


def shifted(value, axis, steps):
    count = lax.axis_size(axis)
    first, last = (max(0, -steps), min(count, count - steps))
    return lax.ppermute(value, axis, [(source, source + steps) for source in range(first, last)])


def rotate(values, positions):
    middle = HD // 2
    frequency = rope_base ** (-(2.0 * jnp.arange(middle, dtype=jnp.float32)) / HD)
    angles = positions.astype(jnp.float32)[:, None] * frequency[None, :]
    cosine = jnp.cos(angles)[:, None, :]
    sine = jnp.sin(angles)[:, None, :]
    front = values[..., :middle]
    behind = values[..., middle:]
    return jnp.concatenate(
        [front * cosine - behind * sine, behind * cosine + front * sine], axis=-1
    )


def segment_info(lengths, indices):
    ends = jnp.cumsum(lengths)
    before = ends[None, :] <= indices[:, None]
    segment = jnp.sum(before.astype(jnp.int32), axis=1)
    start = jnp.sum(jnp.where(before, lengths[None, :], 0), axis=1)
    return (segment, indices - start)


def layer(tokens, kv_weight, queries, lengths, page_owner):
    rows = tokens.shape[0]
    tp_size = lax.axis_size("tp")
    tp_index = lax.axis_index("tp")
    req_index = lax.axis_index("req")
    local_index = req_index * rows + jnp.arange(rows, dtype=jnp.int32)
    segment, positions = segment_info(lengths, local_index)
    local_heads = queries.shape[1] // HD
    partial_value = jnp.dot(tokens, kv_weight, preferred_element_type=jnp.float32)
    pieces = partial_value.reshape(rows, tp_size, HD)
    arrived = lax.all_to_all(jnp.transpose(pieces, (1, 0, 2)), "tp", 0, 0, tiled=True)
    own = jnp.sum(arrived, axis=0)
    is_key = tp_index % 2 == 0
    turned = rotate(own.reshape(rows, 1, HD), positions).reshape(rows, HD)
    mine = jnp.where(is_key, turned, own).astype(jnp.bfloat16)
    other = lax.ppermute(mine, "tp", [(i, i ^ 1) for i in range(tp_size)])
    near = jnp.concatenate([jnp.where(is_key, mine, other), jnp.where(is_key, other, mine)], axis=1)
    rotated = rotate(queries.astype(jnp.float32).reshape(rows, local_heads, HD), positions).astype(
        jnp.bfloat16
    )
    blocks = []
    for distance in range(BACK, 0, -1):
        blocks.append(shifted(near, "req", distance))
    blocks.append(near)
    window = jnp.concatenate(blocks, axis=0)
    key_total = (BACK + 1) * rows
    key_index = (req_index - BACK) * rows + jnp.arange(key_total, dtype=jnp.int32)
    key_segment, _ = segment_info(lengths, key_index)
    allowed = (
        (key_index[None, :] >= 0)
        & (key_index[None, :] <= local_index[:, None])
        & (key_segment[None, :] == segment[:, None])
    )
    key_head = window[:, :HD]
    value_head = window[:, HD:]
    scores = lax.dot_general(
        rotated, key_head, (((2,), (1,)), ((), ())), preferred_element_type=jnp.float32
    ) / math.sqrt(HD)
    scores = jnp.where(allowed[:, None, :], scores, -1e30)
    largest = jnp.max(scores, axis=2, keepdims=True)
    weights = jnp.exp(scores - largest)
    total = jnp.sum(weights, axis=2, keepdims=True)
    mixed = jnp.dot(
        weights.astype(jnp.bfloat16).reshape(rows * local_heads, key_total), value_head,
        preferred_element_type=jnp.float32,
    )
    attended = (mixed / total.reshape(rows * local_heads, 1)).astype(jnp.bfloat16).reshape(rows, local_heads * HD)
    pages_here = page_owner.shape[0]
    owners = page_owner[:, 0]
    page_rows = rows // pages_here
    capacity = 2 * pages_here // lax.axis_size("req")
    order = jnp.arange(pages_here, dtype=jnp.int32)
    earlier = (owners[:, None] == owners[None, :]) & (order[None, :] < order[:, None])
    rank = jnp.sum(earlier.astype(jnp.int32), axis=1)
    target = owners * capacity + rank
    slots = lax.axis_size("req") * capacity
    row_target = (target[:, None] * page_rows + jnp.arange(page_rows, dtype=jnp.int32)[None, :]).reshape(rows)
    placing = (jnp.arange(slots * page_rows, dtype=jnp.int32)[:, None] == row_target[None, :]).astype(jnp.bfloat16)
    outgoing = jnp.dot(placing, mine, preferred_element_type=jnp.float32).astype(jnp.bfloat16)
    cache = lax.all_to_all(outgoing, "req", 0, 0, tiled=True)
    return (attended, cache)


def solution(mesh):
    in_specs = (P("req", "tp"), P("tp", None), P("req", "tp"), P(), P("req", None))
    out_specs = (P("req", "tp"), P("req", "tp"))
    return jax.shard_map(layer, mesh=mesh, in_specs=in_specs, out_specs=out_specs, check_vma=False)
```
